256 devices in a mesh: ctx: 8 (over z_lo, core), head: 8 (over x, z_hi), rep: 4 (over y).
Axes of the slice: x: 4, y: 4, z: 8 (z_hi: 2, z_lo: 4; z = z_hi * 4 + z_lo), core: 2. Of those that a mesh axis runs over, the one named last changes fastest.
Arguments:
- queries: bfloat16 [4, 1024, 8192], P('rep', 'ctx', 'head'), may hold values from -12 to 12
- keys: bfloat16 [4, 1024, 1024], P('rep', 'ctx', 'head'), may hold values from -12 to 12
- values: bfloat16 [4, 1024, 1024], P('rep', 'ctx', 'head'), may hold values from -6 to 6
- grad_out: bfloat16 [4, 1024, 8192], P('rep', 'ctx', 'head'), may hold values from -90 to 90
- segment_ids: int32 [4, 1024], P('rep'), may hold values from 0 to 15, never falling along the last dimension, each value on 1 to 512 neighbouring positions
- head_mask: float32 [64], P('head'), may hold values from 0.25 to 1
- ablated_heads: int32 [8], replicated, may hold values from 0 to 63, as said below
- w_query: bfloat16 [8192, 8192], P(('ctx', 'rep'), 'head'), may hold values from -0.0625 to 0.0625
- w_key: bfloat16 [8192, 1024], P(('ctx', 'rep'), 'head'), may hold values from -0.0625 to 0.0625
- w_value: bfloat16 [8192, 1024], P(('ctx', 'rep'), 'head'), may hold values from -0.0625 to 0.0625
Outputs:
- input_grad: bfloat16 [4, 1024, 8192], P('rep', None, ('ctx', 'head'))
- mask_grad: float32 [64], P('head')
The draws below stay inside these ranges and needn't reach their ends.
Inputs may be any that keep to these rules, and one draw needn't show every extreme that they name: `ablated_heads`: the 8 entries are all different.
All inputs are finite; a program needn't handle non-finite values.
Results may differ from the reference program's by a relative error of at most 0.02.
Values may be sent and summed in bfloat16 or wider, within the bound.
No kernel may reach another device: no remote copies, remote signals or barrier semaphores. Data moves between devices by JAX's collectives and lax.ppermute only.
A program may use at most 128 MiB of HBM per device.

```python
import math
import jax
import jax.numpy as jnp
import numpy as np
from jax import lax

D = 8192
HEADS = 64
KVH = 8
DH = 128
TOK_DEV = 128
NABL = 8
SEQ = 1024
REPS = 4
DOCS = 16
N_HEAD = 8


def draw_queries(key, part):
    shape = (REPS, SEQ, HEADS, DH)
    noise = jnp.clip(jax.random.normal(jax.random.fold_in(key, 1), shape), -6.0, 6.0)
    factor = jnp.exp(jax.random.uniform(jax.random.fold_in(key, 2), (REPS, SEQ, HEADS, 1), minval=math.log(0.6), maxval=math.log(2.0)))
    drawn = noise * factor
    return drawn.reshape(REPS, SEQ, HEADS * DH).astype(jnp.bfloat16)


def draw_keys(key, part):
    shape = (REPS, SEQ, KVH, DH)
    noise = jnp.clip(jax.random.normal(jax.random.fold_in(key, 3), shape), -6.0, 6.0)
    factor = jnp.exp(jax.random.uniform(jax.random.fold_in(key, 4), (REPS, SEQ, KVH, 1), minval=math.log(0.6), maxval=math.log(2.0)))
    drawn = noise * factor
    return drawn.reshape(REPS, SEQ, KVH * DH).astype(jnp.bfloat16)


def draw_grad_out(key, part):
    shape = (REPS, SEQ, HEADS * DH)
    blocks_total = SEQ // TOK_DEV
    place = jnp.arange(SEQ, dtype=jnp.float32)[None, :, None] / SEQ + jnp.arange(REPS, dtype=jnp.float32)[:, None, None] / (REPS * blocks_total)
    noise = jnp.clip(jax.random.normal(jax.random.fold_in(key, 5), shape), -6.0, 6.0)
    rising = jnp.exp(math.log(3.0) * place)
    return (2.0 * noise * rising).astype(jnp.bfloat16)


def draw_ablated_heads(key, part):
    others = jax.random.permutation(jax.random.fold_in(key, 7), HEADS - 1)[:NABL - 1].astype(jnp.int32)
    listed = jnp.concatenate([others, jnp.full((1,), HEADS - 1, jnp.int32)])
    return jax.random.permutation(jax.random.fold_in(key, 8), listed).astype(jnp.int32)


def block_levels(own_key, extent, pieces, low, top_value):
    def one(position, blocks):
        draws = jax.random.uniform(jax.random.fold_in(jax.random.fold_in(own_key, 6), position), (blocks,), jnp.float32, low / len(pieces), top_value / len(pieces))
        return jnp.repeat(jnp.exp(draws), extent[position] // blocks).reshape((-1,) + (1,) * (len(extent) - position - 1))

    factor_of = one(*pieces[0])
    for cut in pieces[1:]:
        factor_of = factor_of * one(*cut)
    return factor_of


def profile(count, total, reach, slope):
    weights = [(1 << 20) // math.isqrt(standing ** slope) + 1 for standing in range(2, count + 1)]
    rest, counts = total - reach - (count - 1), [1] * (count - 1)
    while rest > 0:
        candidates = [i for i in range(count - 1) if counts[i] < reach]
        whole, remaining = sum([weights[i] for i in candidates]), rest
        for i in candidates:
            extra = min(reach - counts[i], max(1, remaining * weights[i] // whole), rest)
            counts[i] = counts[i] + extra
            rest = rest - extra
    return np.array([reach] + counts)


def uneven(rng, count, total, most, skew):
    if count == 2:
        one = jax.random.randint(rng, (), max(1, total - most), min(most, total - 1) + 1)
        return jnp.stack([one, total - one])
    sizes = jnp.asarray(profile(count, total, most, skew), jnp.int32)
    twos = (count - 1) // 2
    source_of, sink = sizes[1:1 + 2 * twos:2], sizes[2:2 + 2 * twos:2]
    slack = jnp.minimum(source_of - 1, most - sink)
    passed = jax.random.randint(jax.random.fold_in(rng, 1), (twos,), 0, 1 << 20) % (slack + 1)
    sizes = sizes.at[1:1 + 2 * twos:2].set(source_of - passed).at[2:2 + 2 * twos:2].set(sink + passed)
    return sizes[jax.random.permutation(jax.random.fold_in(rng, 2), count)]


def bell_draw(own_key, shape, deviation, reach, cuts=(), held_as=jnp.bfloat16):
    level = block_levels(own_key, shape, cuts, -0.22, 0.18) if cuts else 1.0
    values = jax.random.normal(own_key, shape, jnp.float32) * deviation * level
    return jnp.minimum(jnp.maximum(values, -reach), reach).astype(held_as)


def setup_inputs(seed: int = 0) -> dict:
    key_list = jax.random.split(jax.random.key(seed), 11)
    return {
        "queries": draw_queries(jax.random.fold_in(key_list[10], 71), 0),
        "keys": draw_keys(jax.random.fold_in(key_list[10], 71), 0),
        "values": bell_draw(key_list[2], (REPS, SEQ, KVH * DH), 1.0, 6.0, ((0, 4), (1, 8), (2, 8))),
        "grad_out": draw_grad_out(jax.random.fold_in(key_list[10], 71), 0),
        "segment_ids": jax.vmap(lambda own: jnp.searchsorted(jnp.cumsum(uneven(own, DOCS, SEQ, SEQ // 2, 2)), jnp.arange(SEQ), side="right"))(jax.random.split(key_list[4], REPS)).reshape((REPS, SEQ)).astype(jnp.int32),
        "head_mask": jnp.clip(0.25 + 0.75 * jax.random.uniform(key_list[5], (HEADS,), jnp.float32) ** block_levels(key_list[5], (HEADS,), ((0, 8),), -0.2, 0.2), 0.25, 1.0),
        "ablated_heads": draw_ablated_heads(jax.random.fold_in(key_list[10], 71), 0),
        "w_query": bell_draw(key_list[7], (D, HEADS * DH), D ** -0.5, 0.0625, ((0, 32), (1, 8))),
        "w_key": bell_draw(key_list[8], (D, KVH * DH), D ** -0.5, 0.0625, ((0, 32), (1, 8))),
        "w_value": bell_draw(key_list[9], (D, KVH * DH), D ** -0.5, 0.0625, ((0, 32), (1, 8))),
    }


NEG_FILL = -1e+30

def rounded(arr_values):
    return lax.optimization_barrier(arr_values.astype(jnp.bfloat16)).astype(jnp.float32)

def group_terms(group_items, segments):
    query_group, key_group, value_group, grad_group, scale_group = group_items
    length = key_group.shape[0]
    places = jnp.arange(length, dtype=jnp.int32)
    allowed = (places[None, :] <= places[:, None]) & (segments[None, :] == segments[:, None])
    score_scale = 1.0 / math.sqrt(DH)
    query_full = query_group.astype(jnp.float32)
    key_full = key_group.astype(jnp.float32)
    value_full = value_group.astype(jnp.float32)
    scores = jnp.einsum('hic,kc->hik', query_full, key_full) * score_scale
    scores = jnp.where(allowed[None], scores, NEG_FILL)
    row_max = lax.optimization_barrier(jnp.max(scores, axis=-1, keepdims=True))
    exponent = jnp.where(allowed[None], jnp.exp(scores - row_max), 0.0)
    denominator = lax.optimization_barrier(jnp.sum(exponent, axis=-1, keepdims=True))
    log_total = row_max + jnp.log(denominator)
    head_out = (jnp.einsum('hik,kc->hic', rounded(exponent), value_full) / denominator).astype(jnp.bfloat16)
    out_full = head_out.astype(jnp.float32)
    grad_full = grad_group.astype(jnp.float32)
    out_grad = rounded(scale_group[:, None, None] * grad_full)
    out_dot = lax.optimization_barrier(jnp.sum(out_grad * out_full, axis=-1, keepdims=True))
    probability = jnp.where(allowed[None], jnp.exp(scores - log_total), 0.0)
    value_grad = jnp.einsum('hik,hic->kc', rounded(probability), out_grad).astype(jnp.bfloat16)
    prob_grad = jnp.einsum('hic,kc->hik', out_grad, value_full)
    score_grad = rounded(probability * (prob_grad - out_dot))
    query_grad = (jnp.einsum('hik,kc->hic', score_grad, key_full) * score_scale).astype(jnp.bfloat16)
    key_grad = (jnp.einsum('hik,hic->kc', score_grad, query_full) * score_scale).astype(jnp.bfloat16)
    mask_terms = lax.optimization_barrier(jnp.sum(out_full * grad_full, axis=(1, 2)))
    return (query_grad, key_grad, value_grad, mask_terms)

def reference(queries, keys, values, grad_out, segment_ids, head_mask, ablated_heads, w_query, w_key, w_value):
    per_group = HEADS // KVH
    head_ids = jnp.arange(HEADS, dtype=jnp.int32)
    ablate = jnp.any(head_ids[:, None] == ablated_heads[None, :], axis=1)
    head_scale = jnp.where(ablate, 0.0, head_mask).astype(jnp.float32).reshape(KVH, per_group)
    shard_groups = KVH // N_HEAD
    query_cols = shard_groups * per_group * DH
    pair_cols = shard_groups * DH

    def one_prompt(prompt_items):
        query_rows_in, key_rows_in, value_rows_in, grad_rows_in, segments = prompt_items
        query_blocks = query_rows_in.reshape(SEQ, KVH, per_group, DH).transpose(1, 2, 0, 3)
        grad_blocks = grad_rows_in.reshape(SEQ, KVH, per_group, DH).transpose(1, 2, 0, 3)
        key_blocks = key_rows_in.reshape(SEQ, KVH, DH).transpose(1, 0, 2)
        value_blocks = value_rows_in.reshape(SEQ, KVH, DH).transpose(1, 0, 2)
        query_grad, key_grad, value_grad, mask_terms = lax.map(lambda group_items: group_terms(group_items, segments), (query_blocks, key_blocks, value_blocks, grad_blocks, head_scale))
        query_rows = query_grad.transpose(2, 0, 1, 3).reshape(SEQ, HEADS * DH)
        key_rows = key_grad.transpose(1, 0, 2).reshape(SEQ, KVH * DH)
        value_rows = value_grad.transpose(1, 0, 2).reshape(SEQ, KVH * DH)

        def add_shard(carried, shard_index):
            start_query = shard_index * query_cols
            start_pair = shard_index * pair_cols
            product = jnp.dot(lax.dynamic_slice_in_dim(query_rows, start_query, query_cols, 1), lax.dynamic_slice_in_dim(w_query, start_query, query_cols, 1).T, preferred_element_type=jnp.float32)
            product = product + jnp.dot(lax.dynamic_slice_in_dim(key_rows, start_pair, pair_cols, 1), lax.dynamic_slice_in_dim(w_key, start_pair, pair_cols, 1).T, preferred_element_type=jnp.float32)
            product = product + jnp.dot(lax.dynamic_slice_in_dim(value_rows, start_pair, pair_cols, 1), lax.dynamic_slice_in_dim(w_value, start_pair, pair_cols, 1).T, preferred_element_type=jnp.float32)
            return (carried + rounded(product), None)
        summed_rows, unused = lax.scan(add_shard, jnp.zeros((SEQ, D), jnp.float32), jnp.arange(N_HEAD, dtype=jnp.int32))
        return (summed_rows.astype(jnp.bfloat16), mask_terms.reshape(HEADS))
    input_grad, prompt_terms = lax.map(one_prompt, (queries, keys, values, grad_out, segment_ids))
    mask_grad = lax.optimization_barrier(jnp.sum(prompt_terms, axis=0)) / math.sqrt(REPS * SEQ)
    return (input_grad, mask_grad)
```

```python
import math

import jax
import jax.numpy as jnp
from jax import lax
from jax.sharding import PartitionSpec as P

DH = 128


NEG_FILL = -1e30


def on_device(
    queries, keys, values, grad_out, segment_ids, head_mask, ablated_heads, w_query, w_key, w_value
):
    rows_dev = queries.shape[1]
    groups = keys.shape[2] // DH
    local_heads = head_mask.shape[0]
    per_group = local_heads // groups
    block_count = lax.axis_size("ctx")
    my_block = lax.axis_index("ctx")
    seq_len = block_count * rows_dev
    score_scale = 1.0 / math.sqrt(DH)
    all_seg = segment_ids[0]
    query_pos = my_block * rows_dev + jnp.arange(rows_dev, dtype=jnp.int32)
    query_seg = lax.dynamic_slice_in_dim(all_seg, my_block * rows_dev, rows_dev, 0)
    key_pos = jnp.arange(seq_len, dtype=jnp.int32)
    allowed = (key_pos[None, :] <= query_pos[:, None]) & (all_seg[None, :] == query_seg[:, None])

    query_heads = queries[0].reshape(rows_dev, local_heads, DH).transpose(1, 0, 2)
    grad_heads = grad_out[0].reshape(rows_dev, local_heads, DH).transpose(1, 0, 2)
    head_ids = lax.axis_index("head") * local_heads + jnp.arange(local_heads, dtype=jnp.int32)
    ablate = jnp.any(head_ids[:, None] == ablated_heads[None, :], axis=1)
    head_scale = jnp.where(ablate, 0.0, head_mask)

    key_value = lax.all_gather(jnp.stack([keys[0], values[0]]), "ctx", axis=1, tiled=True)
    key_full = key_value[0]
    value_full = key_value[1]

    scores = (
        jnp.einsum("hic,kc->hik", query_heads, key_full, preferred_element_type=jnp.float32)
        * score_scale
    )
    scores = jnp.where(allowed[None], scores, NEG_FILL)
    row_max = jnp.max(scores, axis=-1, keepdims=True)
    exponent = jnp.where(allowed[None], jnp.exp(scores - row_max), 0.0)
    denominator = jnp.sum(exponent, axis=-1, keepdims=True)
    log_total = row_max + jnp.log(denominator)
    weighted = jnp.einsum(
        "hik,kc->hic", exponent.astype(jnp.bfloat16), value_full, preferred_element_type=jnp.float32
    )
    head_out = (weighted / denominator).astype(jnp.bfloat16)
    out_grad = (head_scale[:, None, None] * grad_heads.astype(jnp.float32)).astype(jnp.bfloat16)
    out_dot = jnp.sum(
        out_grad.astype(jnp.float32) * head_out.astype(jnp.float32), axis=-1, keepdims=True
    )
    probability = jnp.where(allowed[None], jnp.exp(scores - log_total), 0.0)
    prob_grad = jnp.einsum(
        "hic,kc->hik", out_grad, value_full, preferred_element_type=jnp.float32
    )
    score_grad = (probability * (prob_grad - out_dot)).astype(jnp.bfloat16)
    value_part = jnp.einsum(
        "hik,hic->kc", probability.astype(jnp.bfloat16), out_grad, preferred_element_type=jnp.float32
    )
    key_part = (
        jnp.einsum("hik,hic->kc", score_grad, query_heads, preferred_element_type=jnp.float32)
        * score_scale
    )
    query_grad = (
        jnp.einsum("hik,kc->hic", score_grad, key_full, preferred_element_type=jnp.float32)
        * score_scale
    ).astype(jnp.bfloat16)
    mask_terms = jnp.sum(
        head_out.astype(jnp.float32) * grad_heads.astype(jnp.float32), axis=(1, 2)
    )

    kv_grad = lax.psum(jnp.stack([key_part, value_part]), "ctx").astype(jnp.bfloat16)
    query_rows = query_grad.transpose(1, 0, 2).reshape(rows_dev, local_heads * DH)
    query_all = lax.all_gather(query_rows, "ctx", axis=0, tiled=True)

    mask_all = lax.all_gather(mask_terms, ("ctx", "rep"), axis=0)
    mask_grad = jnp.sum(mask_all, axis=0) / math.sqrt(lax.axis_size("rep") * seq_len)

    query_piece, key_piece, value_piece = lax.all_gather(
        (w_query, w_key, w_value), "rep", axis=0, tiled=True
    )
    dims = (((1,), (1,)), ((), ()))
    product = lax.dot_general(query_all, query_piece, dims, preferred_element_type=jnp.float32)
    product = product + lax.dot_general(
        kv_grad[0], key_piece, dims, preferred_element_type=jnp.float32
    )
    product = product + lax.dot_general(
        kv_grad[1], value_piece, dims, preferred_element_type=jnp.float32
    )
    partial_value = product.astype(jnp.bfloat16)
    summed = lax.psum_scatter(partial_value, "head", scatter_dimension=1, tiled=True)
    result = summed.reshape(1, seq_len, -1)
    return (result, mask_grad)


def solution(mesh):
    placed = (
        P("rep", "ctx", "head"),
        P("rep", "ctx", "head"),
        P("rep", "ctx", "head"),
        P("rep", "ctx", "head"),
        P("rep", None),
        P("head"),
        P(),
        P(("ctx", "rep"), "head"),
        P(("ctx", "rep"), "head"),
        P(("ctx", "rep"), "head"),
    )
    return jax.shard_map(
        on_device,
        mesh=mesh,
        in_specs=placed,
        out_specs=(P("rep", None, ("ctx", "head")), P("head")),
        check_vma=False,
    )
```

```python
import math

import jax
import jax.numpy as jnp
from jax import lax
from jax.sharding import PartitionSpec as P

DH = 128


NEG_FILL = -1e30


def spread(block, axis):
    count = lax.axis_size(axis)
    copies = jnp.broadcast_to(block[None], (count,) + block.shape)
    return lax.all_to_all(copies, axis, 0, 0, tiled=True)


def on_device(
    queries, keys, values, grad_out, segment_ids, head_mask, ablated_heads, w_query, w_key, w_value
):
    rows_dev = queries.shape[1]
    groups = keys.shape[2] // DH
    local_heads = head_mask.shape[0]
    per_group = local_heads // groups
    block_count = lax.axis_size("ctx")
    my_block = lax.axis_index("ctx")
    seq_len = block_count * rows_dev
    score_scale = 1.0 / math.sqrt(DH)
    all_seg = segment_ids[0]
    query_pos = my_block * rows_dev + jnp.arange(rows_dev, dtype=jnp.int32)
    query_seg = lax.dynamic_slice_in_dim(all_seg, my_block * rows_dev, rows_dev, 0)
    key_pos = jnp.arange(seq_len, dtype=jnp.int32)
    allowed = (key_pos[None, :] <= query_pos[:, None]) & (all_seg[None, :] == query_seg[:, None])

    query_heads = queries[0].reshape(rows_dev, local_heads, DH).transpose(1, 0, 2)
    grad_heads = grad_out[0].reshape(rows_dev, local_heads, DH).transpose(1, 0, 2)
    head_ids = lax.axis_index("head") * local_heads + jnp.arange(local_heads, dtype=jnp.int32)
    ablate = jnp.any(head_ids[:, None] == ablated_heads[None, :], axis=1)
    head_scale = jnp.where(ablate, 0.0, head_mask)

    key_value = spread(jnp.stack([keys[0], values[0]]), "ctx")
    key_full = key_value.transpose(1, 0, 2, 3).reshape(2, seq_len, DH)[0]
    value_full = key_value.transpose(1, 0, 2, 3).reshape(2, seq_len, DH)[1]

    scores = (
        jnp.einsum("hic,kc->hik", query_heads, key_full, preferred_element_type=jnp.float32)
        * score_scale
    )
    scores = jnp.where(allowed[None], scores, NEG_FILL)
    row_max = jnp.max(scores, axis=-1, keepdims=True)
    exponent = jnp.where(allowed[None], jnp.exp(scores - row_max), 0.0)
    denominator = jnp.sum(exponent, axis=-1, keepdims=True)
    log_total = row_max + jnp.log(denominator)
    weighted = jnp.einsum(
        "hik,kc->hic", exponent.astype(jnp.bfloat16), value_full, preferred_element_type=jnp.float32
    )
    head_out = (weighted / denominator).astype(jnp.bfloat16)
    out_grad = (head_scale[:, None, None] * grad_heads.astype(jnp.float32)).astype(jnp.bfloat16)
    out_dot = jnp.sum(
        out_grad.astype(jnp.float32) * head_out.astype(jnp.float32), axis=-1, keepdims=True
    )
    mask_terms = jnp.sum(
        head_out.astype(jnp.float32) * grad_heads.astype(jnp.float32), axis=(1, 2)
    )
    mask_all = spread(mask_terms, ("ctx", "rep"))
    mask_grad = jnp.sum(mask_all, axis=0) / math.sqrt(lax.axis_size("rep") * seq_len)

    probability = jnp.where(allowed[None], jnp.exp(scores - log_total), 0.0)
    prob_grad = jnp.einsum(
        "hic,kc->hik", out_grad, value_full, preferred_element_type=jnp.float32
    )
    score_grad = (probability * (prob_grad - out_dot)).astype(jnp.bfloat16)
    value_part = jnp.einsum(
        "hik,hic->kc", probability.astype(jnp.bfloat16), out_grad, preferred_element_type=jnp.float32
    )
    key_part = (
        jnp.einsum("hik,hic->kc", score_grad, query_heads, preferred_element_type=jnp.float32)
        * score_scale
    )
    query_grad = (
        jnp.einsum("hik,kc->hic", score_grad, key_full, preferred_element_type=jnp.float32)
        * score_scale
    ).astype(jnp.bfloat16)

    kv_parts = jnp.concatenate([key_part, value_part], axis=1).reshape(
        block_count, rows_dev, 2 * DH
    )
    kv_own = jnp.sum(
        lax.all_to_all(kv_parts, "ctx", 0, 0, tiled=True), axis=0
    ).astype(jnp.bfloat16)
    query_rows = query_grad.transpose(1, 0, 2).reshape(rows_dev, local_heads * DH)
    grad_rows = jnp.concatenate([query_rows, kv_own], axis=1)
    grad_all = spread(grad_rows, "ctx").reshape(seq_len, -1)

    weights = jnp.concatenate([w_query, w_key, w_value], axis=1)
    weight_rows = spread(weights, "rep").reshape(-1, weights.shape[1])
    heads_count = lax.axis_size("head")
    weight_rows = weight_rows.reshape(heads_count, -1, weights.shape[1])
    partial_value = jnp.einsum(
        "tk,hdk->htd", grad_all, weight_rows, preferred_element_type=jnp.float32
    ).astype(jnp.bfloat16)
    arrived = lax.all_to_all(partial_value, "head", 0, 0, tiled=True)
    summed = jnp.sum(arrived.astype(jnp.float32), axis=0).astype(jnp.bfloat16)
    result = summed.reshape(1, seq_len, -1)
    return (result, mask_grad)


def solution(mesh):
    placed = (
        P("rep", "ctx", "head"),
        P("rep", "ctx", "head"),
        P("rep", "ctx", "head"),
        P("rep", "ctx", "head"),
        P("rep", None),
        P("head"),
        P(),
        P(("ctx", "rep"), "head"),
        P(("ctx", "rep"), "head"),
        P(("ctx", "rep"), "head"),
    )
    return jax.shard_map(
        on_device,
        mesh=mesh,
        in_specs=placed,
        out_specs=(P("rep", None, ("ctx", "head")), P("head")),
        check_vma=False,
    )
```
